128 devices in a mesh: leaf: 4 (over x), row: 2 (over core), col: 16 (over z, y).
Axes of the slice: x: 4, y: 4, z: 4, core: 2. Of those that a mesh axis runs over, the one named last changes fastest.
Arguments:
- sec_rhs: float32 [4, 7, 64, 2048], P('leaf', None, None, 'row'), may hold values from -6 to 6
- sec_inv: float32 [4, 7, 2048, 2048], P('leaf', None, 'row', 'col'), as said below
- sec_low: float32 [4, 10, 2048, 2048], P('leaf', None, 'row', 'col'), may hold values from -0.09375 to 0.09375
- sec_top: float32 [4, 7, 2048, 2048], P('leaf', None, 'row', 'col'), may hold values from -0.046875 to 0.046875
- sec_rows: int32 [4, 7, 16], P('leaf'), may hold values from 0 to 47, as said below
- top_rhs: float32 [7, 64, 2048], P(None, None, 'row'), may hold values from -6 to 6
- top_inv: float32 [7, 2048, 2048], P(None, 'row', 'col'), as said below
- top_low: float32 [10, 2048, 2048], P(None, 'row', 'col'), may hold values from -0.09375 to 0.09375
- sec_parent: int32 [4], replicated, may hold values from 0 to 3, as said below
- top_parent: int32 [4], replicated, may hold values from 0 to 1, as said below
Outputs:
- sec_sol: float32 [4, 7, 64, 2048], P('leaf', None, None, 'row')
- top_sol: float32 [7, 64, 2048], P(None, None, 'row')
The draws below stay inside these ranges and needn't reach their ends.
Inputs may be any that keep to these rules, and one draw needn't show every extreme that they name: `sec_rows`: within each list the 16 values are distinct. `sec_parent`: each of 0, 1, 2, 3 appears exactly once. `top_parent`: each of 0 and 1 appears exactly twice. `sec_inv`: dense matrices with a positive diagonal; nothing more is promised of their entries. `top_inv`: dense matrices with a positive diagonal; nothing more is promised of their entries.
All inputs are finite; a program needn't handle non-finite values.
Results may differ from the reference program's by a relative error of at most 0.00012.
Values sent between devices are 32-bit elements; how exact they have to be, the bound alone decides.
No kernel may reach another device: no remote copies, remote signals or barrier semaphores. Data moves between devices by JAX's collectives and lax.ppermute only.
A program may use at most 128 MiB of HBM per device.

```python
import math
import jax
import jax.numpy as jnp
from jax import lax

BLOCK = 128
NRHS = 64
NBLK = 16
KEEP = 16
W = 2048
SECTIONS = 4


def dense_inverse(key, leading, width):
    key_off, key_diag = jax.random.split(key)
    full_shape = leading + (width, width)
    spread = 0.5 * jax.random.normal(key_off, full_shape, jnp.float32) / math.sqrt(width)
    diagonal_part = jnp.exp(jax.random.uniform(key_diag, leading + (width,), jnp.float32, -0.69, 0.69))
    row_index = lax.broadcasted_iota(jnp.int32, (width, width), 0)
    col_index = lax.broadcasted_iota(jnp.int32, (width, width), 1)
    return jnp.where(row_index == col_index, diagonal_part[..., :, None], spread)


def draw_sec_inv(key, part):
    return dense_inverse(jax.random.fold_in(key, 101), (SECTIONS, 7), W)


def draw_top_inv(key, part):
    return dense_inverse(jax.random.fold_in(key, 202), (7,), W)


def draw_sec_rows(key, part):
    several = jax.random.split(jax.random.fold_in(key, 303), SECTIONS * 7)
    picks = jax.vmap(lambda single: jax.random.permutation(single, 3 * NBLK))(several)
    return picks[:, :KEEP].reshape(SECTIONS, 7, KEEP).astype(jnp.int32)


def draw_sec_parent(key, part):
    return (jax.random.permutation(jax.random.fold_in(key, 404), SECTIONS) % 4).astype(jnp.int32)


def draw_top_parent(key, part):
    return (jax.random.permutation(jax.random.fold_in(key, 505), 4) % 2).astype(jnp.int32)


def block_levels(own_key, extent, shards, smallest, top_value):
    loudness, own = 1.0, jax.random.fold_in(own_key, 6)
    for axis_at, shards_of in shards:
        draws = jnp.exp(jax.random.uniform(jax.random.fold_in(own, axis_at), (shards_of,), jnp.float32, smallest / len(shards), top_value / len(shards)))
        loudness = loudness * jnp.repeat(draws, extent[axis_at] // shards_of).reshape([-1 if axis == axis_at else 1 for axis in range(len(extent))])
    return loudness


def noise(rng, shape, scale, most, pieces=(), held_as=jnp.bfloat16):
    gain = block_levels(rng, shape, pieces, -0.22, 0.18) if pieces else 1.0
    result = jax.random.normal(rng, shape, jnp.float32) * scale * gain
    return jnp.minimum(jnp.maximum(result, -most), most).astype(held_as)


def setup_inputs(seed: int = 0) -> dict:
    streams_of = jax.random.split(jax.random.key(seed), 11)
    sec_rhs = noise(streams_of[0], (SECTIONS, 7, NRHS, W), 1.0, 6.0, ((0, 4), (3, 2)), jnp.float32)
    sec_inv = draw_sec_inv(jax.random.fold_in(streams_of[10], 71), 0)
    sec_low = noise(streams_of[2], (SECTIONS, 10, W, W), (2 * W) ** -0.5, 0.09375, ((0, 4), (2, 2), (3, 16)), jnp.float32)
    sec_top = noise(streams_of[3], (SECTIONS, 7, KEEP * BLOCK, W), (8 * W) ** -0.5, 0.046875, ((0, 4), (2, 2), (3, 16)), jnp.float32)
    sec_rows = draw_sec_rows(jax.random.fold_in(streams_of[10], 71), 0)
    top_rhs = noise(streams_of[5], (7, NRHS, W), 1.0, 6.0, ((2, 2),), jnp.float32)
    top_inv = draw_top_inv(jax.random.fold_in(streams_of[10], 71), 0)
    top_low = noise(streams_of[7], (10, W, W), (2 * W) ** -0.5, 0.09375, ((1, 2), (2, 16)), jnp.float32)
    sec_parent = draw_sec_parent(jax.random.fold_in(streams_of[10], 71), 0)
    top_parent = draw_top_parent(jax.random.fold_in(streams_of[10], 71), 0)
    return {"sec_rhs": sec_rhs, "sec_inv": sec_inv, "sec_low": sec_low, "sec_top": sec_top, "sec_rows": sec_rows, "top_rhs": top_rhs, "top_inv": top_inv, "top_low": top_low, "sec_parent": sec_parent, "top_parent": top_parent}


def apply_block(vectors, matrices):
    return jnp.einsum("btc,brc->btr", vectors, matrices, precision=lax.Precision.HIGHEST)


def reference(sec_rhs, sec_inv, sec_low, sec_top, sec_rows, top_rhs, top_inv, top_low, sec_parent, top_parent):
    node_ids = jnp.arange(7).astype(jnp.int32)
    block_ids = jnp.arange(NBLK).astype(jnp.int32)
    top_update = jnp.zeros((7, NRHS, W), jnp.float32)
    solved = []
    for section in range(SECTIONS):
        right_side = sec_rhs[section]
        inverse = sec_inv[section]
        lower = sec_low[section]
        sol_leaf = apply_block(right_side[0:4], inverse[0:4])
        upward = apply_block(sol_leaf, lower[0:4])
        acc_mid = upward.reshape(2, 2, NRHS, W).sum(1)
        acc_root = apply_block(sol_leaf, lower[4:8]).sum(0, keepdims=True)
        sol_mid = apply_block(right_side[4:6] - acc_mid, inverse[4:6])
        acc_root = acc_root + apply_block(sol_mid, lower[8:10]).sum(0, keepdims=True)
        sol_root = apply_block(right_side[6:7] - acc_root, inverse[6:7])
        whole = jnp.concatenate([sol_leaf, sol_mid, sol_root], axis=0)
        solved.append(whole)
        contrib = apply_block(whole, sec_top[section]).reshape(7, NRHS, KEEP, BLOCK)
        parent_node = sec_parent[section].astype(jnp.int32)
        grand_node = top_parent[parent_node].astype(jnp.int32)
        path_nodes = jnp.stack([parent_node, grand_node + 4, jnp.int32(6)]).astype(jnp.int32)
        row_list = sec_rows[section].astype(jnp.int32)
        node_of = path_nodes[row_list // NBLK]
        sub_block = row_list % NBLK
        one_hot = ((node_of[:, :, None, None] == node_ids[None, None, :, None])
                   & (sub_block[:, :, None, None] == block_ids[None, None, None, :])).astype(jnp.float32)
        placed = jnp.einsum("jtkl,jknm->ntml", contrib, one_hot, precision=lax.Precision.HIGHEST)
        top_update = top_update + placed.reshape(7, NRHS, W)
    sol_three = apply_block(top_rhs[0:4] - top_update[0:4], top_inv[0:4])
    parent_hot = (top_parent[:, None] == jnp.arange(2)[None, :]).astype(jnp.float32)
    to_mid = apply_block(sol_three, top_low[0:8:2])
    acc_four = jnp.einsum("pq,ptr->qtr", parent_hot, to_mid, precision=lax.Precision.HIGHEST)
    acc_top = apply_block(sol_three, top_low[1:8:2]).sum(0, keepdims=True)
    sol_four = apply_block(top_rhs[4:6] - top_update[4:6] - acc_four, top_inv[4:6])
    acc_top = acc_top + apply_block(sol_four, top_low[8:10]).sum(0, keepdims=True)
    sol_five = apply_block(top_rhs[6:7] - top_update[6:7] - acc_top, top_inv[6:7])
    return jnp.stack(solved, axis=0), jnp.concatenate([sol_three, sol_four, sol_five], axis=0)
```

```python
import jax
import jax.numpy as jnp
from jax import lax
from jax.sharding import PartitionSpec as P

BLOCK = 128


def apply_block(vectors, matrices):
    return jnp.einsum("btc,brc->btr", vectors, matrices, precision=lax.Precision.HIGHEST)


def per_device(
    sec_rhs, sec_inv, sec_low, sec_top, sec_rows, top_rhs, top_inv, top_low, sec_parent, top_parent
):
    here_row = lax.axis_index("row")
    here_col = lax.axis_index("col")
    here_leaf = lax.axis_index("leaf")
    parts_col = lax.axis_size("col")
    parts_leaf = lax.axis_size("leaf")
    rows_here = sec_rhs.shape[-1]
    cols_here = sec_inv.shape[-1]
    per_half = rows_here // cols_here
    nrhs = sec_rhs.shape[2]
    swap = [(0, 1), (1, 0)]

    def to_cols(known):
        at = jnp.clip(here_col - per_half * here_row, 0, per_half - 1)
        mine = lax.dynamic_slice_in_dim(known, at * cols_here, cols_here, 2)
        other = lax.ppermute(mine, "row", swap)
        return jnp.where(here_col // per_half == here_row, mine, other)

    def reduce_to_cols(partial):
        n = partial.shape[0]
        other = lax.ppermute(partial, "row", swap)
        low = jnp.where(here_row == 0, partial, other)
        high = jnp.where(here_row == 0, other, partial)
        full = jnp.concatenate([low, high], axis=2)
        chunks = full.reshape(n, nrhs, parts_col, cols_here).transpose(2, 0, 1, 3)
        got = lax.all_to_all(chunks, "col", 0, 0, tiled=True)
        return got.sum(0)

    def cols_to_rows(cols):
        m = cols.shape[0]
        got = lax.all_gather(cols, "col", axis=0, tiled=False)
        half = lax.dynamic_slice_in_dim(got, here_row * per_half, per_half, 0)
        return half.transpose(1, 2, 0, 3).reshape(m, nrhs, rows_here)

    rhs_cols = to_cols(sec_rhs[0])
    top_rhs_cols = to_cols(top_rhs)
    inverse = sec_inv[0]
    lower = sec_low[0]

    x_leaf = reduce_to_cols(apply_block(rhs_cols[0:4], inverse[0:4]))
    acc_mid = apply_block(x_leaf, lower[0:4]).reshape(2, 2, nrhs, rows_here).sum(1)
    acc_root = apply_block(x_leaf, lower[4:8]).sum(0, keepdims=True)
    y_mid = rhs_cols[4:6] - reduce_to_cols(acc_mid)
    x_mid = reduce_to_cols(apply_block(y_mid, inverse[4:6]))
    acc_root = acc_root + apply_block(x_mid, lower[8:10]).sum(0, keepdims=True)
    y_root = rhs_cols[6:7] - reduce_to_cols(acc_root)
    x_root = reduce_to_cols(apply_block(y_root, inverse[6:7]))
    sec_cols = jnp.concatenate([x_leaf, x_mid, x_root], axis=0)
    sec_out = cols_to_rows(sec_cols)[None]

    block_rows = sec_top.shape[2] // BLOCK
    nblk = rows_here * 2 // BLOCK
    contrib = apply_block(sec_cols, sec_top[0]).reshape(7, nrhs, block_rows, BLOCK)
    mine = lax.dynamic_slice_in_dim(sec_rows[0], here_row * block_rows, block_rows, 1)
    path_ids = jnp.arange(3 * nblk, dtype=jnp.int32)
    one_hot = (mine[:, :, None] == path_ids[None, None, :]).astype(jnp.float32)
    placed = jnp.einsum("ntkl,nkb->btl", contrib, one_hot, precision=lax.Precision.HIGHEST)
    section_ids = jnp.arange(sec_parent.shape[0], dtype=jnp.int32)
    parent_node = jnp.sum(jnp.where(section_ids == here_leaf, sec_parent, 0))
    grand_node = jnp.sum(jnp.where(jnp.arange(4, dtype=jnp.int32) == parent_node, top_parent, 0))
    mid_part = placed[nblk : 2 * nblk]
    zeros = jnp.zeros_like(mid_part)
    spread = jnp.stack(
        [
            placed[0:nblk],
            jnp.where(grand_node == 0, mid_part, zeros),
            jnp.where(grand_node == 1, mid_part, zeros),
            placed[2 * nblk : 3 * nblk],
        ]
    )
    spread = spread + lax.ppermute(spread, "row", swap)
    gathered = lax.all_to_all(spread.transpose(1, 0, 2, 3), "col", 0, 0, tiled=True).sum(0)

    rhs_own = lax.dynamic_index_in_dim(top_rhs_cols, parent_node, 0, keepdims=True)
    inverse_own = lax.dynamic_slice_in_dim(top_inv, parent_node, 1, 0)
    y_three = rhs_own - gathered[0:1]
    x_three = reduce_to_cols(apply_block(y_three, inverse_own))
    payload = jnp.concatenate([x_three, gathered[1:4]], axis=0)
    fanned = jnp.broadcast_to(payload[None], (parts_leaf,) + payload.shape)
    by_leaf = lax.all_to_all(fanned, "leaf", 0, 0, tiled=True)
    upper_update = by_leaf[:, 1:4].sum(0)
    which = sec_parent[None, :] == jnp.arange(4, dtype=jnp.int32)[:, None]
    x_by_leaf = by_leaf[:, 0]
    sol_three = jnp.sum(jnp.where(which[:, :, None, None], x_by_leaf[None], 0.0), axis=1)

    to_mid = apply_block(sol_three, top_low[0:8:2])
    parent_hot = top_parent[:, None] == jnp.arange(2, dtype=jnp.int32)[None, :]
    acc_four = jnp.sum(jnp.where(parent_hot.T[:, :, None, None], to_mid[None], 0.0), axis=1)
    acc_top = apply_block(sol_three, top_low[1:8:2]).sum(0, keepdims=True)
    y_four = top_rhs_cols[4:6] - upper_update[0:2] - reduce_to_cols(acc_four)
    x_four = reduce_to_cols(apply_block(y_four, top_inv[4:6]))
    rows_early = cols_to_rows(jnp.concatenate([sol_three, x_four], axis=0))
    acc_top = acc_top + apply_block(x_four, top_low[8:10]).sum(0, keepdims=True)
    y_five = top_rhs_cols[6:7] - upper_update[2:3] - reduce_to_cols(acc_top)
    x_five = reduce_to_cols(apply_block(y_five, top_inv[6:7]))
    top_out = jnp.concatenate([rows_early, cols_to_rows(x_five)], axis=0)
    return (sec_out, top_out)


def solution(mesh):
    placed = (
        P("leaf", None, None, "row"),
        P("leaf", None, "row", "col"),
        P("leaf", None, "row", "col"),
        P("leaf", None, "row", "col"),
        P("leaf", None, None),
        P(None, None, "row"),
        P(None, "row", "col"),
        P(None, "row", "col"),
        P(),
        P(),
    )
    return jax.shard_map(
        per_device,
        mesh=mesh,
        in_specs=placed,
        out_specs=(P("leaf", None, None, "row"), P(None, None, "row")),
        check_vma=False,
    )
```

```python
import jax
import jax.numpy as jnp
from jax import lax
from jax.sharding import PartitionSpec as P

BLOCK = 128


def apply_block(vectors, matrices):
    return jnp.einsum("btc,brc->btr", vectors, matrices, precision=lax.Precision.HIGHEST)


def per_device(
    sec_rhs, sec_inv, sec_low, sec_top, sec_rows, top_rhs, top_inv, top_low, sec_parent, top_parent
):
    here_row = lax.axis_index("row")
    here_col = lax.axis_index("col")
    here_leaf = lax.axis_index("leaf")
    parts_col = lax.axis_size("col")
    parts_leaf = lax.axis_size("leaf")
    rows_here = sec_rhs.shape[-1]
    cols_here = sec_inv.shape[-1]
    per_half = rows_here // cols_here
    nrhs = sec_rhs.shape[2]
    swap = [(0, 1), (1, 0)]

    def to_cols(known):
        at = jnp.clip(here_col - per_half * here_row, 0, per_half - 1)
        mine = lax.dynamic_slice_in_dim(known, at * cols_here, cols_here, 2)
        other = lax.ppermute(mine, "row", swap)
        return jnp.where(here_col // per_half == here_row, mine, other)

    def reduce_to_cols(partial):
        n = partial.shape[0]
        half_t = nrhs // 2
        keep = lax.dynamic_slice_in_dim(partial, here_row * half_t, half_t, 1)
        give = lax.dynamic_slice_in_dim(partial, (1 - here_row) * half_t, half_t, 1)
        got = lax.ppermute(give, "row", swap)
        low = jnp.where(here_row == 0, keep, got)
        high = jnp.where(here_row == 0, got, keep)
        full = jnp.concatenate([low, high], axis=2)
        chunks = full.reshape(n, half_t, parts_col, cols_here).transpose(2, 0, 1, 3)
        red = lax.all_to_all(chunks, "col", 0, 0, tiled=True).sum(0)
        return join_halves(red)

    def join_halves(red):
        other = lax.ppermute(red, "row", swap)
        first = jnp.where(here_row == 0, red, other)
        second = jnp.where(here_row == 0, other, red)
        return jnp.concatenate([first, second], axis=1)

    def reduce_to_rows(partial):
        n = partial.shape[0]
        piece = rows_here // parts_col
        chunks = partial.reshape(n, nrhs, parts_col, piece).transpose(2, 0, 1, 3)
        red = lax.all_to_all(chunks, "col", 0, 0, tiled=True).sum(0)
        fanned = jnp.broadcast_to(red[None], (parts_col,) + red.shape)
        got = lax.all_to_all(fanned, "col", 0, 0, tiled=True)
        return got.transpose(1, 2, 0, 3).reshape(n, nrhs, rows_here)

    def cols_to_rows(cols):
        m = cols.shape[0]
        got = lax.all_gather(cols, "col", axis=0, tiled=False)
        half = lax.dynamic_slice_in_dim(got, here_row * per_half, per_half, 0)
        return half.transpose(1, 2, 0, 3).reshape(m, nrhs, rows_here)

    rhs_cols = to_cols(sec_rhs[0])
    top_rhs_cols = to_cols(top_rhs)
    inverse = sec_inv[0]
    lower = sec_low[0]

    x_leaf = reduce_to_cols(apply_block(rhs_cols[0:4], inverse[0:4]))
    acc_mid = apply_block(x_leaf, lower[0:4]).reshape(2, 2, nrhs, rows_here).sum(1)
    acc_root = apply_block(x_leaf, lower[4:8]).sum(0, keepdims=True)
    y_mid = rhs_cols[4:6] - reduce_to_cols(acc_mid)
    x_mid = reduce_to_cols(apply_block(y_mid, inverse[4:6]))
    acc_root = acc_root + apply_block(x_mid, lower[8:10]).sum(0, keepdims=True)
    y_root = rhs_cols[6:7] - reduce_to_cols(acc_root)
    x_root = reduce_to_cols(apply_block(y_root, inverse[6:7]))
    sec_cols = jnp.concatenate([x_leaf, x_mid, x_root], axis=0)
    sec_out = cols_to_rows(sec_cols)[None]

    block_rows = sec_top.shape[2] // BLOCK
    nblk = rows_here * 2 // BLOCK
    contrib = apply_block(sec_cols, sec_top[0]).reshape(7, nrhs, block_rows, BLOCK)
    mine = lax.dynamic_slice_in_dim(sec_rows[0], here_row * block_rows, block_rows, 1)
    path_ids = jnp.arange(3 * nblk, dtype=jnp.int32)
    one_hot = (mine[:, :, None] == path_ids[None, None, :]).astype(jnp.float32)
    placed = jnp.einsum("ntkl,nkb->btl", contrib, one_hot, precision=lax.Precision.HIGHEST)
    section_ids = jnp.arange(sec_parent.shape[0], dtype=jnp.int32)
    parent_node = jnp.sum(jnp.where(section_ids == here_leaf, sec_parent, 0))
    half_t = nrhs // 2
    spread = placed.reshape(3, nblk, nrhs, BLOCK)
    keep = lax.dynamic_slice_in_dim(spread, here_row * half_t, half_t, 2)
    give = lax.dynamic_slice_in_dim(spread, (1 - here_row) * half_t, half_t, 2)
    spread = keep + lax.ppermute(give, "row", swap)
    gathered = lax.all_to_all(spread.transpose(1, 0, 2, 3), "col", 0, 0, tiled=True).sum(0)
    gathered = join_halves(gathered)
    rhs_own = lax.dynamic_index_in_dim(top_rhs_cols, parent_node, 0, keepdims=True)
    inverse_own = lax.dynamic_slice_in_dim(top_inv, parent_node, 1, 0)
    y_three = rhs_own - gathered[0:1]
    x_three = reduce_to_cols(apply_block(y_three, inverse_own))
    payload = jnp.concatenate([x_three, gathered[1:3]], axis=0)
    fanned = jnp.broadcast_to(payload[None], (parts_leaf,) + payload.shape)
    by_leaf = lax.all_to_all(fanned, "leaf", 0, 0, tiled=True)
    grand_of = jnp.sum(jnp.where(sec_parent[:, None] == jnp.arange(4, dtype=jnp.int32)[None, :], top_parent[None, :], 0), axis=1)
    mid_hot = grand_of[None, :] == jnp.arange(2, dtype=jnp.int32)[:, None]
    upd_four = jnp.sum(jnp.where(mid_hot[:, :, None, None], by_leaf[None, :, 1], 0.0), axis=1)
    upd_five = by_leaf[:, 2:3].sum(0)
    which = sec_parent[None, :] == jnp.arange(4, dtype=jnp.int32)[:, None]
    x_by_leaf = by_leaf[:, 0]
    sol_three = jnp.sum(jnp.where(which[:, :, None, None], x_by_leaf[None], 0.0), axis=1)

    to_mid = apply_block(sol_three, top_low[0:8:2])
    parent_hot = top_parent[:, None] == jnp.arange(2, dtype=jnp.int32)[None, :]
    acc_four = jnp.sum(jnp.where(parent_hot.T[:, :, None, None], to_mid[None], 0.0), axis=1)
    acc_top = apply_block(sol_three, top_low[1:8:2]).sum(0, keepdims=True)
    y_four = top_rhs_cols[4:6] - upd_four - reduce_to_cols(acc_four)
    x_four = reduce_to_cols(apply_block(y_four, top_inv[4:6]))
    rows_early = cols_to_rows(jnp.concatenate([sol_three, x_four], axis=0))
    acc_top = acc_top + apply_block(x_four, top_low[8:10]).sum(0, keepdims=True)
    y_five = top_rhs_cols[6:7] - upd_five - reduce_to_cols(acc_top)
    rows_five = reduce_to_rows(apply_block(y_five, top_inv[6:7]))
    top_out = jnp.concatenate([rows_early, rows_five], axis=0)
    return (sec_out, top_out)


def solution(mesh):
    placed = (
        P("leaf", None, None, "row"),
        P("leaf", None, "row", "col"),
        P("leaf", None, "row", "col"),
        P("leaf", None, "row", "col"),
        P("leaf", None, None),
        P(None, None, "row"),
        P(None, "row", "col"),
        P(None, "row", "col"),
        P(),
        P(),
    )
    return jax.shard_map(
        per_device,
        mesh=mesh,
        in_specs=placed,
        out_specs=(P("leaf", None, None, "row"), P(None, None, "row")),
        check_vma=False,
    )
```

```python
import jax
import jax.numpy as jnp
from jax import lax
from jax.sharding import PartitionSpec as P

BLOCK = 128


def apply_block(vectors, matrices):
    return jnp.einsum("btc,brc->btr", vectors, matrices, precision=lax.Precision.HIGH)


def per_device(
    sec_rhs, sec_inv, sec_low, sec_top, sec_rows, top_rhs, top_inv, top_low, sec_parent, top_parent
):
    here_row = lax.axis_index("row")
    here_col = lax.axis_index("col")
    here_leaf = lax.axis_index("leaf")
    parts_col = lax.axis_size("col")
    parts_leaf = lax.axis_size("leaf")
    rows_here = sec_rhs.shape[-1]
    cols_here = sec_inv.shape[-1]
    per_half = rows_here // cols_here
    nrhs = sec_rhs.shape[2]
    swap = [(0, 1), (1, 0)]

    def to_cols(known):
        at = jnp.clip(here_col - per_half * here_row, 0, per_half - 1)
        mine = lax.dynamic_slice_in_dim(known, at * cols_here, cols_here, 2)
        other = lax.ppermute(mine, "row", swap)
        return jnp.where(here_col // per_half == here_row, mine, other)

    def reduce_to_cols(partial):
        n = partial.shape[0]
        half_t = nrhs // 2
        keep = lax.dynamic_slice_in_dim(partial, here_row * half_t, half_t, 1)
        give = lax.dynamic_slice_in_dim(partial, (1 - here_row) * half_t, half_t, 1)
        got = lax.ppermute(give, "row", swap)
        low = jnp.where(here_row == 0, keep, got)
        high = jnp.where(here_row == 0, got, keep)
        full = jnp.concatenate([low, high], axis=2)
        chunks = full.reshape(n, half_t, parts_col, cols_here).transpose(2, 0, 1, 3)
        red = lax.all_to_all(chunks, "col", 0, 0, tiled=True).sum(0)
        return join_halves(red)

    def join_halves(red):
        other = lax.ppermute(red, "row", swap)
        first = jnp.where(here_row == 0, red, other)
        second = jnp.where(here_row == 0, other, red)
        return jnp.concatenate([first, second], axis=1)

    def reduce_to_rows(partial):
        n = partial.shape[0]
        piece = rows_here // parts_col
        chunks = partial.reshape(n, nrhs, parts_col, piece).transpose(2, 0, 1, 3)
        red = lax.all_to_all(chunks, "col", 0, 0, tiled=True).sum(0)
        fanned = jnp.broadcast_to(red[None], (parts_col,) + red.shape)
        got = lax.all_to_all(fanned, "col", 0, 0, tiled=True)
        return got.transpose(1, 2, 0, 3).reshape(n, nrhs, rows_here)

    def cols_to_rows(cols):
        m = cols.shape[0]
        got = lax.all_gather(cols, "col", axis=0, tiled=False)
        half = lax.dynamic_slice_in_dim(got, here_row * per_half, per_half, 0)
        return half.transpose(1, 2, 0, 3).reshape(m, nrhs, rows_here)

    rhs_cols = to_cols(sec_rhs[0])
    top_rhs_cols = to_cols(top_rhs)
    inverse = sec_inv[0]
    lower = sec_low[0]

    x_leaf = reduce_to_cols(apply_block(rhs_cols[0:4], inverse[0:4]))
    acc_mid = apply_block(x_leaf, lower[0:4]).reshape(2, 2, nrhs, rows_here).sum(1)
    acc_root = apply_block(x_leaf, lower[4:8]).sum(0, keepdims=True)
    y_mid = rhs_cols[4:6] - reduce_to_cols(acc_mid)
    x_mid = reduce_to_cols(apply_block(y_mid, inverse[4:6]))
    acc_root = acc_root + apply_block(x_mid, lower[8:10]).sum(0, keepdims=True)
    y_root = rhs_cols[6:7] - reduce_to_cols(acc_root)
    x_root = reduce_to_cols(apply_block(y_root, inverse[6:7]))
    sec_cols = jnp.concatenate([x_leaf, x_mid, x_root], axis=0)
    sec_out = cols_to_rows(sec_cols)[None]

    block_rows = sec_top.shape[2] // BLOCK
    nblk = rows_here * 2 // BLOCK
    contrib = apply_block(sec_cols, sec_top[0]).reshape(7, nrhs, block_rows, BLOCK)
    mine = lax.dynamic_slice_in_dim(sec_rows[0], here_row * block_rows, block_rows, 1)
    path_ids = jnp.arange(3 * nblk, dtype=jnp.int32)
    one_hot = (mine[:, :, None] == path_ids[None, None, :]).astype(jnp.float32)
    placed = jnp.einsum("ntkl,nkb->btl", contrib, one_hot, precision=lax.Precision.HIGHEST)
    section_ids = jnp.arange(sec_parent.shape[0], dtype=jnp.int32)
    parent_node = jnp.sum(jnp.where(section_ids == here_leaf, sec_parent, 0))
    half_t = nrhs // 2
    spread = placed.reshape(3, nblk, nrhs, BLOCK)
    keep = lax.dynamic_slice_in_dim(spread, here_row * half_t, half_t, 2)
    give = lax.dynamic_slice_in_dim(spread, (1 - here_row) * half_t, half_t, 2)
    spread = keep + lax.ppermute(give, "row", swap)
    gathered = lax.all_to_all(spread.transpose(1, 0, 2, 3), "col", 0, 0, tiled=True).sum(0)
    gathered = join_halves(gathered)
    rhs_own = lax.dynamic_index_in_dim(top_rhs_cols, parent_node, 0, keepdims=True)
    inverse_own = lax.dynamic_slice_in_dim(top_inv, parent_node, 1, 0)
    y_three = rhs_own - gathered[0:1]
    x_three = reduce_to_cols(apply_block(y_three, inverse_own))
    payload = jnp.concatenate([x_three, gathered[1:3]], axis=0)
    fanned = jnp.broadcast_to(payload[None], (parts_leaf,) + payload.shape)
    by_leaf = lax.all_to_all(fanned, "leaf", 0, 0, tiled=True)
    grand_of = jnp.sum(jnp.where(sec_parent[:, None] == jnp.arange(4, dtype=jnp.int32)[None, :], top_parent[None, :], 0), axis=1)
    mid_hot = grand_of[None, :] == jnp.arange(2, dtype=jnp.int32)[:, None]
    upd_four = jnp.sum(jnp.where(mid_hot[:, :, None, None], by_leaf[None, :, 1], 0.0), axis=1)
    upd_five = by_leaf[:, 2:3].sum(0)
    which = sec_parent[None, :] == jnp.arange(4, dtype=jnp.int32)[:, None]
    x_by_leaf = by_leaf[:, 0]
    sol_three = jnp.sum(jnp.where(which[:, :, None, None], x_by_leaf[None], 0.0), axis=1)

    to_mid = apply_block(sol_three, top_low[0:8:2])
    parent_hot = top_parent[:, None] == jnp.arange(2, dtype=jnp.int32)[None, :]
    acc_four = jnp.sum(jnp.where(parent_hot.T[:, :, None, None], to_mid[None], 0.0), axis=1)
    acc_top = apply_block(sol_three, top_low[1:8:2]).sum(0, keepdims=True)
    y_four = top_rhs_cols[4:6] - upd_four - reduce_to_cols(acc_four)
    x_four = reduce_to_cols(apply_block(y_four, top_inv[4:6]))
    rows_early = cols_to_rows(jnp.concatenate([sol_three, x_four], axis=0))
    acc_top = acc_top + apply_block(x_four, top_low[8:10]).sum(0, keepdims=True)
    sec_out, acc_top = lax.optimization_barrier((sec_out, acc_top))
    y_five = top_rhs_cols[6:7] - upd_five - reduce_to_cols(acc_top)
    part_five = apply_block(y_five, top_inv[6:7])
    rows_early, part_five = lax.optimization_barrier((rows_early, part_five))
    rows_five = reduce_to_rows(part_five)
    top_out = jnp.concatenate([rows_early, rows_five], axis=0)
    return (sec_out, top_out)


def solution(mesh):
    placed = (
        P("leaf", None, None, "row"),
        P("leaf", None, "row", "col"),
        P("leaf", None, "row", "col"),
        P("leaf", None, "row", "col"),
        P("leaf", None, None),
        P(None, None, "row"),
        P(None, "row", "col"),
        P(None, "row", "col"),
        P(),
        P(),
    )
    return jax.shard_map(
        per_device,
        mesh=mesh,
        in_specs=placed,
        out_specs=(P("leaf", None, None, "row"), P(None, None, "row")),
        check_vma=False,
    )
```

```python
import jax
import jax.numpy as jnp
from jax import lax
from jax.sharding import PartitionSpec as P

BLOCK = 128


def apply_block(vectors, matrices):
    return jnp.einsum("btc,brc->btr", vectors, matrices, precision=lax.Precision.HIGHEST)


def per_device(
    sec_rhs, sec_inv, sec_low, sec_top, sec_rows, top_rhs, top_inv, top_low, sec_parent, top_parent
):
    here_row = lax.axis_index("row")
    here_col = lax.axis_index("col")
    here_leaf = lax.axis_index("leaf")
    parts_col = lax.axis_size("col")
    parts_row = lax.axis_size("row")
    parts_leaf = lax.axis_size("leaf")
    rows_here = sec_rhs.shape[-1]
    cols_here = sec_inv.shape[-1]
    per_half = rows_here // cols_here
    nrhs = sec_rhs.shape[2]
    half_t = nrhs // 2
    swap = [(0, 1), (1, 0)]

    def to_half_cols(known):
        at = jnp.clip(here_col - per_half * here_row, 0, per_half - 1)
        mine = lax.dynamic_slice_in_dim(known, at * cols_here, cols_here, 2)
        other = lax.ppermute(mine, "row", swap)
        cols = jnp.where(here_col // per_half == here_row, mine, other)
        return lax.dynamic_slice_in_dim(cols, here_row * half_t, half_t, 1)

    def partner(matrices):
        return lax.ppermute(matrices, "row", swap)

    def full_product(vectors, own, other):
        a = apply_block(vectors, own)
        b = apply_block(vectors, other)
        low = jnp.where(here_row == 0, a, b)
        high = jnp.where(here_row == 0, b, a)
        return jnp.concatenate([low, high], axis=2)

    def reduce_to_cols(full):
        n = full.shape[0]
        chunks = full.reshape(n, half_t, parts_col, cols_here).transpose(2, 0, 1, 3)
        return lax.all_to_all(chunks, "col", 0, 0, tiled=True).sum(0)

    def assemble(got):
        m = got.shape[2]
        half = lax.dynamic_slice_in_dim(got, here_row * per_half, per_half, 1)
        return half.transpose(2, 0, 3, 1, 4).reshape(m, nrhs, rows_here)

    def gather_rows(pieces):
        got = lax.all_gather(pieces, ("row", "col"), axis=0, tiled=False)
        return assemble(got.reshape((parts_row, parts_col) + pieces.shape))

    def fan_rows(pieces):
        fanned = jnp.broadcast_to(pieces[None], (parts_row * parts_col,) + pieces.shape)
        got = lax.all_to_all(fanned, ("row", "col"), 0, 0, tiled=True)
        return assemble(got.reshape((parts_row, parts_col) + pieces.shape))

    rhs_half = to_half_cols(sec_rhs[0])
    top_rhs_half = to_half_cols(top_rhs)
    inverse = sec_inv[0]
    lower = sec_low[0]
    inverse_o = partner(inverse)
    lower_o = partner(lower)
    keep_o = partner(sec_top[0])
    top_inv_o = partner(top_inv)
    top_low_o = partner(top_low)

    x_leaf = reduce_to_cols(full_product(rhs_half[0:4], inverse[0:4], inverse_o[0:4]))
    width = 2 * rows_here
    acc_mid = full_product(x_leaf, lower[0:4], lower_o[0:4]).reshape(2, 2, half_t, width).sum(1)
    acc_root = full_product(x_leaf, lower[4:8], lower_o[4:8]).sum(0, keepdims=True)
    y_mid = rhs_half[4:6] - reduce_to_cols(acc_mid)
    x_mid = reduce_to_cols(full_product(y_mid, inverse[4:6], inverse_o[4:6]))
    acc_root = acc_root + full_product(x_mid, lower[8:10], lower_o[8:10]).sum(0, keepdims=True)
    y_root = rhs_half[6:7] - reduce_to_cols(acc_root)
    x_root = reduce_to_cols(full_product(y_root, inverse[6:7], inverse_o[6:7]))
    sec_half = jnp.concatenate([x_leaf, x_mid, x_root], axis=0)
    sec_out = gather_rows(sec_half)[None]

    keep_blocks = sec_top.shape[2] * parts_row // BLOCK
    nblk = width // BLOCK
    contrib = full_product(sec_half, sec_top[0], keep_o).reshape(7, half_t, keep_blocks, BLOCK)
    path_ids = jnp.arange(3 * nblk, dtype=jnp.int32)
    one_hot = (sec_rows[0][:, :, None] == path_ids[None, None, :]).astype(jnp.float32)
    placed = jnp.einsum("ntkl,nkb->btl", contrib, one_hot, precision=lax.Precision.HIGHEST)
    spread = placed.reshape(3, nblk, half_t, BLOCK)
    gathered = lax.all_to_all(spread.transpose(1, 0, 2, 3), "col", 0, 0, tiled=True).sum(0)

    section_ids = jnp.arange(sec_parent.shape[0], dtype=jnp.int32)
    parent_node = jnp.sum(jnp.where(section_ids == here_leaf, sec_parent, 0))
    rhs_own = lax.dynamic_index_in_dim(top_rhs_half, parent_node, 0, keepdims=True)
    inverse_own = lax.dynamic_slice_in_dim(top_inv, parent_node, 1, 0)
    inverse_own_o = lax.dynamic_slice_in_dim(top_inv_o, parent_node, 1, 0)
    y_three = rhs_own - gathered[0:1]
    x_three = reduce_to_cols(full_product(y_three, inverse_own, inverse_own_o))
    payload = jnp.concatenate([x_three, gathered[1:3]], axis=0)
    fanned = jnp.broadcast_to(payload[None], (parts_leaf,) + payload.shape)
    by_leaf = lax.all_to_all(fanned, "leaf", 0, 0, tiled=True)
    node_ids = jnp.arange(4, dtype=jnp.int32)
    grand_of = jnp.sum(jnp.where(sec_parent[:, None] == node_ids[None, :], top_parent[None, :], 0), axis=1)
    mid_hot = grand_of[None, :] == jnp.arange(2, dtype=jnp.int32)[:, None]
    upd_four = jnp.sum(jnp.where(mid_hot[:, :, None, None], by_leaf[None, :, 1], 0.0), axis=1)
    upd_five = by_leaf[:, 2:3].sum(0)
    which = sec_parent[None, :] == node_ids[:, None]
    sol_three = jnp.sum(jnp.where(which[:, :, None, None], by_leaf[None, :, 0], 0.0), axis=1)

    to_mid = full_product(sol_three, top_low[0:8:2], top_low_o[0:8:2])
    parent_hot = top_parent[:, None] == jnp.arange(2, dtype=jnp.int32)[None, :]
    acc_four = jnp.sum(jnp.where(parent_hot.T[:, :, None, None], to_mid[None], 0.0), axis=1)
    acc_top = full_product(sol_three, top_low[1:8:2], top_low_o[1:8:2]).sum(0, keepdims=True)
    y_four = top_rhs_half[4:6] - upd_four - reduce_to_cols(acc_four)
    x_four = reduce_to_cols(full_product(y_four, top_inv[4:6], top_inv_o[4:6]))
    rows_early = gather_rows(jnp.concatenate([sol_three, x_four], axis=0))
    acc_top = acc_top + full_product(x_four, top_low[8:10], top_low_o[8:10]).sum(0, keepdims=True)
    sec_out, acc_top = lax.optimization_barrier((sec_out, acc_top))
    y_five = top_rhs_half[6:7] - upd_five - reduce_to_cols(acc_top)
    x_five = reduce_to_cols(full_product(y_five, top_inv[6:7], top_inv_o[6:7]))
    top_out = jnp.concatenate([rows_early, fan_rows(x_five)], axis=0)
    return (sec_out, top_out)


def solution(mesh):
    placed = (
        P("leaf", None, None, "row"),
        P("leaf", None, "row", "col"),
        P("leaf", None, "row", "col"),
        P("leaf", None, "row", "col"),
        P("leaf", None, None),
        P(None, None, "row"),
        P(None, "row", "col"),
        P(None, "row", "col"),
        P(),
        P(),
    )
    return jax.shard_map(
        per_device,
        mesh=mesh,
        in_specs=placed,
        out_specs=(P("leaf", None, None, "row"), P(None, None, "row")),
        check_vma=False,
    )
```

```python
import jax
import jax.numpy as jnp
from jax import lax
from jax.sharding import PartitionSpec as P

BLOCK = 128


def apply_block(vectors, matrices):
    return jnp.einsum("btc,brc->btr", vectors, matrices, precision=lax.Precision.HIGHEST)


def per_device(
    sec_rhs, sec_inv, sec_low, sec_top, sec_rows, top_rhs, top_inv, top_low, sec_parent, top_parent
):
    here_row = lax.axis_index("row")
    here_col = lax.axis_index("col")
    here_leaf = lax.axis_index("leaf")
    parts_col = lax.axis_size("col")
    parts_leaf = lax.axis_size("leaf")
    rows_here = sec_rhs.shape[-1]
    cols_here = sec_inv.shape[-1]
    per_half = rows_here // cols_here
    nrhs = sec_rhs.shape[2]
    swap = [(0, 1), (1, 0)]

    def to_cols(known):
        at = jnp.clip(here_col - per_half * here_row, 0, per_half - 1)
        mine = lax.dynamic_slice_in_dim(known, at * cols_here, cols_here, 2)
        other = lax.ppermute(mine, "row", swap)
        return jnp.where(here_col // per_half == here_row, mine, other)

    def reduce_to_cols(partial):
        n = partial.shape[0]
        half_t = nrhs // 2
        keep = lax.dynamic_slice_in_dim(partial, here_row * half_t, half_t, 1)
        give = lax.dynamic_slice_in_dim(partial, (1 - here_row) * half_t, half_t, 1)
        got = lax.ppermute(give, "row", swap)
        low = jnp.where(here_row == 0, keep, got)
        high = jnp.where(here_row == 0, got, keep)
        full = jnp.concatenate([low, high], axis=2)
        chunks = full.reshape(n, half_t, parts_col, cols_here).transpose(2, 0, 1, 3)
        red = lax.all_to_all(chunks, "col", 0, 0, tiled=True).sum(0)
        return join_halves(red)

    def join_halves(red):
        other = lax.ppermute(red, "row", swap)
        first = jnp.where(here_row == 0, red, other)
        second = jnp.where(here_row == 0, other, red)
        return jnp.concatenate([first, second], axis=1)

    def reduce_to_rows(partial):
        n = partial.shape[0]
        piece = rows_here // parts_col
        chunks = partial.reshape(n, nrhs, parts_col, piece).transpose(2, 0, 1, 3)
        red = lax.all_to_all(chunks, "col", 0, 0, tiled=True).sum(0)
        fanned = jnp.broadcast_to(red[None], (parts_col,) + red.shape)
        got = lax.all_to_all(fanned, "col", 0, 0, tiled=True)
        return got.transpose(1, 2, 0, 3).reshape(n, nrhs, rows_here)

    def cols_to_rows(cols):
        m = cols.shape[0]
        got = lax.all_gather(cols, "col", axis=0, tiled=False)
        half = lax.dynamic_slice_in_dim(got, here_row * per_half, per_half, 0)
        return half.transpose(1, 2, 0, 3).reshape(m, nrhs, rows_here)

    rhs_cols = to_cols(sec_rhs[0])
    top_rhs_cols = to_cols(top_rhs)
    inverse = sec_inv[0]
    lower = sec_low[0]

    x_leaf = reduce_to_cols(apply_block(rhs_cols[0:4], inverse[0:4]))
    acc_mid = apply_block(x_leaf, lower[0:4]).reshape(2, 2, nrhs, rows_here).sum(1)
    acc_root = apply_block(x_leaf, lower[4:8]).sum(0, keepdims=True)
    y_mid = rhs_cols[4:6] - reduce_to_cols(acc_mid)
    x_mid = reduce_to_cols(apply_block(y_mid, inverse[4:6]))
    acc_root = acc_root + apply_block(x_mid, lower[8:10]).sum(0, keepdims=True)
    y_root = rhs_cols[6:7] - reduce_to_cols(acc_root)
    x_root = reduce_to_cols(apply_block(y_root, inverse[6:7]))
    sec_cols = jnp.concatenate([x_leaf, x_mid, x_root], axis=0)
    sec_out = cols_to_rows(sec_cols)[None]

    block_rows = sec_top.shape[2] // BLOCK
    nblk = rows_here * 2 // BLOCK
    contrib = apply_block(sec_cols, sec_top[0]).reshape(7, nrhs, block_rows, BLOCK)
    mine = lax.dynamic_slice_in_dim(sec_rows[0], here_row * block_rows, block_rows, 1)
    path_ids = jnp.arange(3 * nblk, dtype=jnp.int32)
    one_hot = (mine[:, :, None] == path_ids[None, None, :]).astype(jnp.float32)
    placed = jnp.einsum("ntkl,nkb->btl", contrib, one_hot, precision=lax.Precision.HIGHEST)
    section_ids = jnp.arange(sec_parent.shape[0], dtype=jnp.int32)
    parent_node = jnp.sum(jnp.where(section_ids == here_leaf, sec_parent, 0))
    half_t = nrhs // 2
    spread = placed.reshape(3, nblk, nrhs, BLOCK)
    keep = lax.dynamic_slice_in_dim(spread, here_row * half_t, half_t, 2)
    give = lax.dynamic_slice_in_dim(spread, (1 - here_row) * half_t, half_t, 2)
    spread = keep + lax.ppermute(give, "row", swap)
    gathered = lax.all_to_all(spread.transpose(1, 0, 2, 3), "col", 0, 0, tiled=True).sum(0)
    gathered = join_halves(gathered)
    rhs_own = lax.dynamic_index_in_dim(top_rhs_cols, parent_node, 0, keepdims=True)
    inverse_own = lax.dynamic_slice_in_dim(top_inv, parent_node, 1, 0)
    y_three = rhs_own - gathered[0:1]
    x_three = reduce_to_cols(apply_block(y_three, inverse_own))
    payload = jnp.concatenate([x_three, gathered[1:3]], axis=0)
    fanned = jnp.broadcast_to(payload[None], (parts_leaf,) + payload.shape)
    by_leaf = lax.all_to_all(fanned, "leaf", 0, 0, tiled=True)
    grand_of = jnp.sum(jnp.where(sec_parent[:, None] == jnp.arange(4, dtype=jnp.int32)[None, :], top_parent[None, :], 0), axis=1)
    mid_hot = grand_of[None, :] == jnp.arange(2, dtype=jnp.int32)[:, None]
    upd_four = jnp.sum(jnp.where(mid_hot[:, :, None, None], by_leaf[None, :, 1], 0.0), axis=1)
    upd_five = by_leaf[:, 2:3].sum(0)
    which = sec_parent[None, :] == jnp.arange(4, dtype=jnp.int32)[:, None]
    x_by_leaf = by_leaf[:, 0]
    sol_three = jnp.sum(jnp.where(which[:, :, None, None], x_by_leaf[None], 0.0), axis=1)

    to_mid = apply_block(sol_three, top_low[0:8:2])
    parent_hot = top_parent[:, None] == jnp.arange(2, dtype=jnp.int32)[None, :]
    acc_four = jnp.sum(jnp.where(parent_hot.T[:, :, None, None], to_mid[None], 0.0), axis=1)
    acc_top = apply_block(sol_three, top_low[1:8:2]).sum(0, keepdims=True)
    y_four = top_rhs_cols[4:6] - upd_four - reduce_to_cols(acc_four)
    x_four = reduce_to_cols(apply_block(y_four, top_inv[4:6]))
    rows_early = cols_to_rows(jnp.concatenate([sol_three, x_four], axis=0))
    acc_top = acc_top + apply_block(x_four, top_low[8:10]).sum(0, keepdims=True)
    sec_out, acc_top = lax.optimization_barrier((sec_out, acc_top))
    y_five = top_rhs_cols[6:7] - upd_five - reduce_to_cols(acc_top)
    rows_five = reduce_to_rows(apply_block(y_five, top_inv[6:7]))
    top_out = jnp.concatenate([rows_early, rows_five], axis=0)
    return (sec_out, top_out)


def solution(mesh):
    placed = (
        P("leaf", None, None, "row"),
        P("leaf", None, "row", "col"),
        P("leaf", None, "row", "col"),
        P("leaf", None, "row", "col"),
        P("leaf", None, None),
        P(None, None, "row"),
        P(None, "row", "col"),
        P(None, "row", "col"),
        P(),
        P(),
    )
    return jax.shard_map(
        per_device,
        mesh=mesh,
        in_specs=placed,
        out_specs=(P("leaf", None, None, "row"), P(None, None, "row")),
        check_vma=False,
    )
```

```python
import jax
import jax.numpy as jnp
from jax import lax
from jax.sharding import PartitionSpec as P

BLOCK = 128


def apply_block(vectors, matrices):
    return jnp.einsum("btc,brc->btr", vectors, matrices, precision=lax.Precision.HIGHEST)


def per_device(
    sec_rhs, sec_inv, sec_low, sec_top, sec_rows, top_rhs, top_inv, top_low, sec_parent, top_parent
):
    here_row = lax.axis_index("row")
    here_col = lax.axis_index("col")
    here_leaf = lax.axis_index("leaf")
    parts_col = lax.axis_size("col")
    parts_leaf = lax.axis_size("leaf")
    rows_here = sec_rhs.shape[-1]
    cols_here = sec_inv.shape[-1]
    per_half = rows_here // cols_here
    nrhs = sec_rhs.shape[2]
    swap = [(0, 1), (1, 0)]

    def to_cols(known):
        at = jnp.clip(here_col - per_half * here_row, 0, per_half - 1)
        mine = lax.dynamic_slice_in_dim(known, at * cols_here, cols_here, 2)
        other = lax.ppermute(mine, "row", swap)
        return jnp.where(here_col // per_half == here_row, mine, other)

    def reduce_to_cols(partial):
        n = partial.shape[0]
        half_t = nrhs // 2
        keep = lax.dynamic_slice_in_dim(partial, here_row * half_t, half_t, 1)
        give = lax.dynamic_slice_in_dim(partial, (1 - here_row) * half_t, half_t, 1)
        got = lax.ppermute(give, "row", swap)
        low = jnp.where(here_row == 0, keep, got)
        high = jnp.where(here_row == 0, got, keep)
        full = jnp.concatenate([low, high], axis=2)
        chunks = full.reshape(n, half_t, parts_col, cols_here).transpose(2, 0, 1, 3)
        red = lax.all_to_all(chunks, "col", 0, 0, tiled=True).sum(0)
        return join_halves(red)

    def join_halves(red):
        other = lax.ppermute(red, "row", swap)
        first = jnp.where(here_row == 0, red, other)
        second = jnp.where(here_row == 0, other, red)
        return jnp.concatenate([first, second], axis=1)

    def reduce_to_rows(partial):
        n = partial.shape[0]
        piece = rows_here // parts_col
        chunks = partial.reshape(n, nrhs, parts_col, piece).transpose(2, 0, 1, 3)
        red = lax.all_to_all(chunks, "col", 0, 0, tiled=True).sum(0)
        fanned = jnp.broadcast_to(red[None], (parts_col,) + red.shape)
        got = lax.all_to_all(fanned, "col", 0, 0, tiled=True)
        return got.transpose(1, 2, 0, 3).reshape(n, nrhs, rows_here)

    def cols_to_rows(cols):
        m = cols.shape[0]
        received = []
        for shift in range(per_half):
            pairs = []
            for b in range(parts_col):
                for k in range(2):
                    to = (b // per_half) * parts_col + (b % per_half - shift) % per_half + per_half * k
                    pairs.append((k * parts_col + b, to))
            received.append(lax.ppermute(cols, ("row", "col"), pairs))
        twice = jnp.stack(received + received)
        start = (per_half - here_col % per_half) % per_half
        ordered = lax.dynamic_slice_in_dim(twice, start, per_half, 0)
        return ordered.transpose(1, 2, 0, 3).reshape(m, nrhs, rows_here)

    rhs_cols = to_cols(sec_rhs[0])
    top_rhs_cols = to_cols(top_rhs)
    inverse = sec_inv[0]
    lower = sec_low[0]

    x_leaf = reduce_to_cols(apply_block(rhs_cols[0:4], inverse[0:4]))
    acc_mid = apply_block(x_leaf, lower[0:4]).reshape(2, 2, nrhs, rows_here).sum(1)
    acc_root = apply_block(x_leaf, lower[4:8]).sum(0, keepdims=True)
    y_mid = rhs_cols[4:6] - reduce_to_cols(acc_mid)
    x_mid = reduce_to_cols(apply_block(y_mid, inverse[4:6]))
    acc_root = acc_root + apply_block(x_mid, lower[8:10]).sum(0, keepdims=True)
    y_root = rhs_cols[6:7] - reduce_to_cols(acc_root)
    x_root = reduce_to_cols(apply_block(y_root, inverse[6:7]))
    sec_cols = jnp.concatenate([x_leaf, x_mid, x_root], axis=0)
    sec_out = cols_to_rows(sec_cols)[None]

    block_rows = sec_top.shape[2] // BLOCK
    nblk = rows_here * 2 // BLOCK
    contrib = apply_block(sec_cols, sec_top[0]).reshape(7, nrhs, block_rows, BLOCK)
    mine = lax.dynamic_slice_in_dim(sec_rows[0], here_row * block_rows, block_rows, 1)
    path_ids = jnp.arange(3 * nblk, dtype=jnp.int32)
    one_hot = (mine[:, :, None] == path_ids[None, None, :]).astype(jnp.float32)
    placed = jnp.einsum("ntkl,nkb->btl", contrib, one_hot, precision=lax.Precision.HIGHEST)
    section_ids = jnp.arange(sec_parent.shape[0], dtype=jnp.int32)
    parent_node = jnp.sum(jnp.where(section_ids == here_leaf, sec_parent, 0))
    half_t = nrhs // 2
    spread = placed.reshape(3, nblk, nrhs, BLOCK)
    keep = lax.dynamic_slice_in_dim(spread, here_row * half_t, half_t, 2)
    give = lax.dynamic_slice_in_dim(spread, (1 - here_row) * half_t, half_t, 2)
    spread = keep + lax.ppermute(give, "row", swap)
    gathered = lax.all_to_all(spread.transpose(1, 0, 2, 3), "col", 0, 0, tiled=True).sum(0)
    gathered = join_halves(gathered)
    rhs_own = lax.dynamic_index_in_dim(top_rhs_cols, parent_node, 0, keepdims=True)
    inverse_own = lax.dynamic_slice_in_dim(top_inv, parent_node, 1, 0)
    y_three = rhs_own - gathered[0:1]
    x_three = reduce_to_cols(apply_block(y_three, inverse_own))
    payload = jnp.concatenate([x_three, gathered[1:3]], axis=0)
    fanned = jnp.broadcast_to(payload[None], (parts_leaf,) + payload.shape)
    by_leaf = lax.all_to_all(fanned, "leaf", 0, 0, tiled=True)
    grand_of = jnp.sum(jnp.where(sec_parent[:, None] == jnp.arange(4, dtype=jnp.int32)[None, :], top_parent[None, :], 0), axis=1)
    mid_hot = grand_of[None, :] == jnp.arange(2, dtype=jnp.int32)[:, None]
    upd_four = jnp.sum(jnp.where(mid_hot[:, :, None, None], by_leaf[None, :, 1], 0.0), axis=1)
    upd_five = by_leaf[:, 2:3].sum(0)
    which = sec_parent[None, :] == jnp.arange(4, dtype=jnp.int32)[:, None]
    x_by_leaf = by_leaf[:, 0]
    sol_three = jnp.sum(jnp.where(which[:, :, None, None], x_by_leaf[None], 0.0), axis=1)

    to_mid = apply_block(sol_three, top_low[0:8:2])
    parent_hot = top_parent[:, None] == jnp.arange(2, dtype=jnp.int32)[None, :]
    acc_four = jnp.sum(jnp.where(parent_hot.T[:, :, None, None], to_mid[None], 0.0), axis=1)
    acc_top = apply_block(sol_three, top_low[1:8:2]).sum(0, keepdims=True)
    y_four = top_rhs_cols[4:6] - upd_four - reduce_to_cols(acc_four)
    x_four = reduce_to_cols(apply_block(y_four, top_inv[4:6]))
    rows_early = cols_to_rows(jnp.concatenate([sol_three, x_four], axis=0))
    acc_top = acc_top + apply_block(x_four, top_low[8:10]).sum(0, keepdims=True)
    sec_out, acc_top = lax.optimization_barrier((sec_out, acc_top))
    y_five = top_rhs_cols[6:7] - upd_five - reduce_to_cols(acc_top)
    rows_five = reduce_to_rows(apply_block(y_five, top_inv[6:7]))
    top_out = jnp.concatenate([rows_early, rows_five], axis=0)
    return (sec_out, top_out)


def solution(mesh):
    placed = (
        P("leaf", None, None, "row"),
        P("leaf", None, "row", "col"),
        P("leaf", None, "row", "col"),
        P("leaf", None, "row", "col"),
        P("leaf", None, None),
        P(None, None, "row"),
        P(None, "row", "col"),
        P(None, "row", "col"),
        P(),
        P(),
    )
    return jax.shard_map(
        per_device,
        mesh=mesh,
        in_specs=placed,
        out_specs=(P("leaf", None, None, "row"), P(None, None, "row")),
        check_vma=False,
    )
```

```python
import jax
import jax.numpy as jnp
from jax import lax
from jax.sharding import PartitionSpec as P

BLOCK = 128


def apply_block(vectors, matrices):
    return jnp.einsum("btc,brc->btr", vectors, matrices, precision=lax.Precision.HIGHEST)


def solve(
    sec_rhs, sec_inv, sec_low, sec_top, sec_rows, top_rhs, top_inv, top_low, sec_parent, top_parent
):
    here_row = lax.axis_index("row")
    here_col = lax.axis_index("col")
    here_leaf = lax.axis_index("leaf")
    parts_col = lax.axis_size("col")
    parts_leaf = lax.axis_size("leaf")
    rows_here = sec_rhs.shape[-1]
    cols_here = sec_inv.shape[-1]
    per_half = rows_here // cols_here
    nrhs = sec_rhs.shape[2]
    swap = [(0, 1), (1, 0)]

    def to_cols(known):
        at = jnp.clip(here_col - per_half * here_row, 0, per_half - 1)
        mine = lax.dynamic_slice_in_dim(known, at * cols_here, cols_here, 2)
        other = lax.ppermute(mine, "row", swap)
        return jnp.where(here_col // per_half == here_row, mine, other)

    def reduce_to_cols(partial):
        n = partial.shape[0]
        half_t = nrhs // 2
        keep = lax.dynamic_slice_in_dim(partial, here_row * half_t, half_t, 1)
        give = lax.dynamic_slice_in_dim(partial, (1 - here_row) * half_t, half_t, 1)
        got = lax.ppermute(give, "row", swap)
        low = jnp.where(here_row == 0, keep, got)
        high = jnp.where(here_row == 0, got, keep)
        full = jnp.concatenate([low, high], axis=2)
        chunks = full.reshape(n, half_t, parts_col, cols_here).transpose(2, 0, 1, 3)
        got = lax.all_to_all(chunks, "col", 0, 0, tiled=True)
        return join_halves(got.sum(0))

    def join_halves(red):
        other = lax.ppermute(red, "row", swap)
        first = jnp.where(here_row == 0, red, other)
        second = jnp.where(here_row == 0, other, red)
        return jnp.concatenate([first, second], axis=1)

    def reduce_to_rows(partial):
        n = partial.shape[0]
        piece = rows_here // parts_col
        chunks = partial.reshape(n, nrhs, parts_col, piece).transpose(2, 0, 1, 3)
        red = lax.all_to_all(chunks, "col", 0, 0, tiled=True).sum(0)
        fanned = jnp.broadcast_to(red[None], (parts_col,) + red.shape)
        got = lax.all_to_all(fanned, "col", 0, 0, tiled=True)
        return got.transpose(1, 2, 0, 3).reshape(n, nrhs, rows_here)

    def cols_to_rows(cols):
        m = cols.shape[0]
        got = lax.all_gather(cols, "col", axis=0, tiled=False)
        half = lax.dynamic_slice_in_dim(got, here_row * per_half, per_half, 0)
        return half.transpose(1, 2, 0, 3).reshape(m, nrhs, rows_here)

    rhs_cols = to_cols(sec_rhs[0])
    top_rhs_cols = to_cols(top_rhs)
    inverse = sec_inv[0]
    lower = sec_low[0]

    x_leaf = reduce_to_cols(apply_block(rhs_cols[0:4], inverse[0:4]))
    acc_mid = apply_block(x_leaf, lower[0:4]).reshape(2, 2, nrhs, rows_here).sum(1)
    acc_root = apply_block(x_leaf, lower[4:8]).sum(0, keepdims=True)
    acc_root = lax.optimization_barrier(acc_root)
    y_mid = rhs_cols[4:6] - reduce_to_cols(acc_mid)
    early = apply_block(x_leaf, sec_top[0][0:4])
    x_mid = reduce_to_cols(apply_block(y_mid, inverse[4:6]))
    acc_root = acc_root + apply_block(x_mid, lower[8:10]).sum(0, keepdims=True)
    y_root = rhs_cols[6:7] - reduce_to_cols(acc_root)
    x_root = reduce_to_cols(apply_block(y_root, inverse[6:7]))
    sec_cols = jnp.concatenate([x_leaf, x_mid, x_root], axis=0)
    sec_out = cols_to_rows(sec_cols)[None]

    block_rows = sec_top.shape[2] // BLOCK
    nblk = rows_here * 2 // BLOCK
    mine = lax.dynamic_slice_in_dim(sec_rows[0], here_row * block_rows, block_rows, 1)
    path_ids = jnp.arange(3 * nblk, dtype=jnp.int32)
    one_hot = (mine[:, :, None] == path_ids[None, None, :]).astype(jnp.float32)
    middle = apply_block(x_mid, sec_top[0][4:6])
    early = jnp.concatenate([early, middle], axis=0).reshape(6, nrhs, block_rows, BLOCK)
    placed = jnp.einsum("ntkl,nkb->btl", early, one_hot[0:6], precision=lax.Precision.HIGHEST)
    late = apply_block(x_root, sec_top[0][6:7]).reshape(1, nrhs, block_rows, BLOCK)
    placed = placed + jnp.einsum("ntkl,nkb->btl", late, one_hot[6:7], precision=lax.Precision.HIGHEST)
    section_ids = jnp.arange(sec_parent.shape[0], dtype=jnp.int32)
    parent_node = jnp.sum(jnp.where(section_ids == here_leaf, sec_parent, 0))
    half_t = nrhs // 2
    spread = placed.reshape(3, nblk, nrhs, BLOCK)
    keep = lax.dynamic_slice_in_dim(spread, here_row * half_t, half_t, 2)
    give = lax.dynamic_slice_in_dim(spread, (1 - here_row) * half_t, half_t, 2)
    spread = keep + lax.ppermute(give, "row", swap)
    gathered = lax.all_to_all(spread.transpose(1, 0, 2, 3), "col", 0, 0, tiled=True).sum(0)
    gathered = join_halves(gathered)
    rhs_own = lax.dynamic_index_in_dim(top_rhs_cols, parent_node, 0, keepdims=True)
    inverse_own = lax.dynamic_slice_in_dim(top_inv, parent_node, 1, 0)
    y_three = rhs_own - gathered[0:1]
    x_three = reduce_to_cols(apply_block(y_three, inverse_own))
    payload = jnp.concatenate([x_three, gathered[1:3]], axis=0)
    fanned = jnp.broadcast_to(payload[None], (parts_leaf,) + payload.shape)
    by_leaf = lax.all_to_all(fanned, "leaf", 0, 0, tiled=True)
    grand_of = jnp.sum(jnp.where(sec_parent[:, None] == jnp.arange(4, dtype=jnp.int32)[None, :], top_parent[None, :], 0), axis=1)
    mid_hot = grand_of[None, :] == jnp.arange(2, dtype=jnp.int32)[:, None]
    upd_four = jnp.sum(jnp.where(mid_hot[:, :, None, None], by_leaf[None, :, 1], 0.0), axis=1)
    upd_five = by_leaf[:, 2:3].sum(0)
    which = sec_parent[None, :] == jnp.arange(4, dtype=jnp.int32)[:, None]
    x_by_leaf = by_leaf[:, 0]
    sol_three = jnp.sum(jnp.where(which[:, :, None, None], x_by_leaf[None], 0.0), axis=1)

    to_mid = apply_block(sol_three, top_low[0:8:2])
    parent_hot = top_parent[:, None] == jnp.arange(2, dtype=jnp.int32)[None, :]
    acc_four = jnp.sum(jnp.where(parent_hot.T[:, :, None, None], to_mid[None], 0.0), axis=1)
    acc_top = apply_block(sol_three, top_low[1:8:2]).sum(0, keepdims=True)
    y_four = top_rhs_cols[4:6] - upd_four - reduce_to_cols(acc_four)
    x_four = reduce_to_cols(apply_block(y_four, top_inv[4:6]))
    rows_early = cols_to_rows(jnp.concatenate([sol_three, x_four], axis=0))
    acc_top = acc_top + apply_block(x_four, top_low[8:10]).sum(0, keepdims=True)
    sec_out, acc_top = lax.optimization_barrier((sec_out, acc_top))
    y_five = top_rhs_cols[6:7] - upd_five - reduce_to_cols(acc_top)
    rows_five = reduce_to_rows(apply_block(y_five, top_inv[6:7]))
    top_out = jnp.concatenate([rows_early, rows_five], axis=0)
    return (sec_out, top_out)


def solution(mesh):
    placed = (
        P("leaf", None, None, "row"),
        P("leaf", None, "row", "col"),
        P("leaf", None, "row", "col"),
        P("leaf", None, "row", "col"),
        P("leaf", None, None),
        P(None, None, "row"),
        P(None, "row", "col"),
        P(None, "row", "col"),
        P(),
        P(),
    )
    return jax.shard_map(
        solve,
        mesh=mesh,
        in_specs=placed,
        out_specs=(P("leaf", None, None, "row"), P(None, None, "row")),
        check_vma=False,
    )
```

```python
import jax
import jax.numpy as jnp
from jax import lax
from jax.sharding import PartitionSpec as P

BLOCK = 128


def apply_block(vectors, matrices):
    return jnp.einsum("btc,brc->btr", vectors, matrices, precision=lax.Precision.HIGHEST)


def solve(
    sec_rhs, sec_inv, sec_low, sec_top, sec_rows, top_rhs, top_inv, top_low, sec_parent, top_parent
):
    here_row = lax.axis_index("row")
    here_col = lax.axis_index("col")
    here_leaf = lax.axis_index("leaf")
    parts_col = lax.axis_size("col")
    parts_leaf = lax.axis_size("leaf")
    rows_here = sec_rhs.shape[-1]
    cols_here = sec_inv.shape[-1]
    per_half = rows_here // cols_here
    nrhs = sec_rhs.shape[2]
    swap = [(0, 1), (1, 0)]

    def to_cols(known):
        at = jnp.clip(here_col - per_half * here_row, 0, per_half - 1)
        mine = lax.dynamic_slice_in_dim(known, at * cols_here, cols_here, 2)
        other = lax.ppermute(mine, "row", swap)
        return jnp.where(here_col // per_half == here_row, mine, other)

    def reduce_to_cols(partial):
        n = partial.shape[0]
        half_t = nrhs // 2
        keep = lax.dynamic_slice_in_dim(partial, here_row * half_t, half_t, 1)
        give = lax.dynamic_slice_in_dim(partial, (1 - here_row) * half_t, half_t, 1)
        got = lax.ppermute(give, "row", swap)
        low = jnp.where(here_row == 0, keep, got)
        high = jnp.where(here_row == 0, got, keep)
        full = jnp.concatenate([low, high], axis=2)
        chunks = full.reshape(n, half_t, parts_col, cols_here).transpose(2, 0, 1, 3)
        got = lax.all_to_all(chunks, "col", 0, 0, tiled=True)
        return join_halves(got.sum(0))

    def join_halves(red):
        other = lax.ppermute(red, "row", swap)
        first = jnp.where(here_row == 0, red, other)
        second = jnp.where(here_row == 0, other, red)
        return jnp.concatenate([first, second], axis=1)

    def reduce_to_rows(partial):
        n = partial.shape[0]
        piece = rows_here // parts_col
        tile = (nrhs * piece // cols_here, cols_here)
        chunks = partial.reshape(n, nrhs, parts_col, piece).transpose(2, 0, 1, 3)
        chunks = chunks.reshape((parts_col, n) + tile)
        red = lax.all_to_all(chunks, "col", 0, 0, tiled=True).sum(0)
        fanned = jnp.broadcast_to(red[None], (parts_col,) + red.shape)
        got = lax.all_to_all(fanned, "col", 0, 0, tiled=True)
        got = got.reshape(parts_col, n, nrhs, piece)
        return got.transpose(1, 2, 0, 3).reshape(n, nrhs, rows_here)

    def cols_to_rows(cols):
        m = cols.shape[0]
        got = lax.all_gather(cols, "col", axis=0, tiled=False)
        half = lax.dynamic_slice_in_dim(got, here_row * per_half, per_half, 0)
        return half.transpose(1, 2, 0, 3).reshape(m, nrhs, rows_here)

    rhs_cols = to_cols(sec_rhs[0])
    top_rhs_cols = to_cols(top_rhs)
    inverse = sec_inv[0]
    lower = sec_low[0]

    x_leaf = reduce_to_cols(apply_block(rhs_cols[0:4], inverse[0:4]))
    acc_mid = apply_block(x_leaf, lower[0:4]).reshape(2, 2, nrhs, rows_here).sum(1)
    acc_root = apply_block(x_leaf, lower[4:8]).sum(0, keepdims=True)
    acc_root = lax.optimization_barrier(acc_root)
    y_mid = rhs_cols[4:6] - reduce_to_cols(acc_mid)
    x_mid = reduce_to_cols(apply_block(y_mid, inverse[4:6]))
    acc_root = acc_root + apply_block(x_mid, lower[8:10]).sum(0, keepdims=True)
    y_root = rhs_cols[6:7] - reduce_to_cols(acc_root)
    x_root = reduce_to_cols(apply_block(y_root, inverse[6:7]))
    sec_cols = jnp.concatenate([x_leaf, x_mid, x_root], axis=0)
    sec_out = cols_to_rows(sec_cols)[None]

    block_rows = sec_top.shape[2] // BLOCK
    nblk = rows_here * 2 // BLOCK
    mine = lax.dynamic_slice_in_dim(sec_rows[0], here_row * block_rows, block_rows, 1)
    path_ids = jnp.arange(3 * nblk, dtype=jnp.int32)
    one_hot = (mine[:, :, None] == path_ids[None, None, :]).astype(jnp.float32)
    early = apply_block(sec_cols[0:6], sec_top[0][0:6]).reshape(6, nrhs, block_rows, BLOCK)
    placed = jnp.einsum("ntkl,nkb->btl", early, one_hot[0:6], precision=lax.Precision.HIGHEST)
    late = apply_block(x_root, sec_top[0][6:7]).reshape(1, nrhs, block_rows, BLOCK)
    placed = placed + jnp.einsum("ntkl,nkb->btl", late, one_hot[6:7], precision=lax.Precision.HIGHEST)
    section_ids = jnp.arange(sec_parent.shape[0], dtype=jnp.int32)
    parent_node = jnp.sum(jnp.where(section_ids == here_leaf, sec_parent, 0))
    half_t = nrhs // 2
    spread = placed.reshape(3, nblk, nrhs, BLOCK)
    keep = lax.dynamic_slice_in_dim(spread, here_row * half_t, half_t, 2)
    give = lax.dynamic_slice_in_dim(spread, (1 - here_row) * half_t, half_t, 2)
    spread = keep + lax.ppermute(give, "row", swap)
    gathered = lax.all_to_all(spread.transpose(1, 0, 2, 3), "col", 0, 0, tiled=True).sum(0)
    gathered = join_halves(gathered)
    rhs_own = lax.dynamic_index_in_dim(top_rhs_cols, parent_node, 0, keepdims=True)
    inverse_own = lax.dynamic_slice_in_dim(top_inv, parent_node, 1, 0)
    y_three = rhs_own - gathered[0:1]
    x_three = reduce_to_cols(apply_block(y_three, inverse_own))
    payload = jnp.concatenate([x_three, gathered[1:3]], axis=0)
    fanned = jnp.broadcast_to(payload[None], (parts_leaf,) + payload.shape)
    by_leaf = lax.all_to_all(fanned, "leaf", 0, 0, tiled=True)
    grand_of = jnp.sum(jnp.where(sec_parent[:, None] == jnp.arange(4, dtype=jnp.int32)[None, :], top_parent[None, :], 0), axis=1)
    mid_hot = grand_of[None, :] == jnp.arange(2, dtype=jnp.int32)[:, None]
    upd_four = jnp.sum(jnp.where(mid_hot[:, :, None, None], by_leaf[None, :, 1], 0.0), axis=1)
    upd_five = by_leaf[:, 2:3].sum(0)
    which = sec_parent[None, :] == jnp.arange(4, dtype=jnp.int32)[:, None]
    x_by_leaf = by_leaf[:, 0]
    sol_three = jnp.sum(jnp.where(which[:, :, None, None], x_by_leaf[None], 0.0), axis=1)

    to_mid = apply_block(sol_three, top_low[0:8:2])
    parent_hot = top_parent[:, None] == jnp.arange(2, dtype=jnp.int32)[None, :]
    acc_four = jnp.sum(jnp.where(parent_hot.T[:, :, None, None], to_mid[None], 0.0), axis=1)
    acc_top = apply_block(sol_three, top_low[1:8:2]).sum(0, keepdims=True)
    y_four = top_rhs_cols[4:6] - upd_four - reduce_to_cols(acc_four)
    x_four = reduce_to_cols(apply_block(y_four, top_inv[4:6]))
    rows_early = cols_to_rows(jnp.concatenate([sol_three, x_four], axis=0))
    acc_top = acc_top + apply_block(x_four, top_low[8:10]).sum(0, keepdims=True)
    sec_out, acc_top = lax.optimization_barrier((sec_out, acc_top))
    y_five = top_rhs_cols[6:7] - upd_five - reduce_to_cols(acc_top)
    rows_five = reduce_to_rows(apply_block(y_five, top_inv[6:7]))
    top_out = jnp.concatenate([rows_early, rows_five], axis=0)
    return (sec_out, top_out)


def solution(mesh):
    placed = (
        P("leaf", None, None, "row"),
        P("leaf", None, "row", "col"),
        P("leaf", None, "row", "col"),
        P("leaf", None, "row", "col"),
        P("leaf", None, None),
        P(None, None, "row"),
        P(None, "row", "col"),
        P(None, "row", "col"),
        P(),
        P(),
    )
    return jax.shard_map(
        solve,
        mesh=mesh,
        in_specs=placed,
        out_specs=(P("leaf", None, None, "row"), P(None, None, "row")),
        check_vma=False,
    )
```
